128 devices in a mesh: seq: 32 (over y, z, core), head: 4 (over x).
Axes of the slice: x: 4, y: 4, z: 4, core: 2. Of those that a mesh axis runs over, the one named last changes fastest.
Arguments:
- queries: bfloat16 [16384, 2048], P('seq', 'head'), may hold values from -6 to 6
- key_pairs: bfloat16 [16384, 2, 2048], P('seq', None, 'head'), may hold values from -6 to 6
- value_pairs: bfloat16 [16384, 2, 2048], P('seq', None, 'head'), may hold values from -0.1875 to 0.1875
- init_state: float32 [16, 128, 128], P('head'), may hold values from -6 to 6
- out_weight: bfloat16 [2048, 2048], replicated, may hold values from -0.125 to 0.125
Outputs:
- projected: bfloat16 [16384, 2048], P('seq', 'head')
The draws below stay inside these ranges and needn't reach their ends.
All inputs are finite; a program needn't handle non-finite values.
Results may differ from the reference program's by a relative error of at most 0.0085.
Values may be sent and summed in bfloat16 or wider, within the bound.
No kernel may reach another device: no remote copies, remote signals or barrier semaphores. Data moves between devices by JAX's collectives and lax.ppermute only.
A program may use at most 128 MiB of HBM per device.

```python
import jax
import jax.numpy as jnp
from jax import lax

DMODEL = 2048
HEADS = 16
HEAD_DIM = 128
BLOCK = 32
TOKENS = 16384


def levels(stream_key, dims, cuts, least, high):
    gain, own = 1.0, jax.random.fold_in(stream_key, 6)
    for dim, shards_of in cuts:
        heights = jnp.exp(jax.random.uniform(jax.random.fold_in(own, dim), (shards_of,), jnp.float32, least / len(cuts), high / len(cuts)))
        gain = gain * jnp.repeat(heights, dims[dim] // shards_of).reshape([-1 if axis == dim else 1 for axis in range(len(dims))])
    return gain


def scatter_about(key, extent, width, most, cuts=(), kind=jnp.bfloat16):
    values = jax.random.normal(key, extent, jnp.float32) * width
    if len(cuts) > 0:
        values = levels(key, extent, cuts, -0.22, 0.18) * values
    return jnp.clip(values, min=-most, max=most).astype(kind)


def setup_inputs(seed: int = 0) -> dict:
    splits = jax.random.split(jax.random.key(seed), 6)
    return {
        "queries": scatter_about(splits[0], (TOKENS, HEADS * HEAD_DIM), 1.0, 6.0, ((0, 32), (1, 4))),
        "key_pairs": scatter_about(splits[1], (TOKENS, 2, HEADS * HEAD_DIM), 1.0, 6.0, ((0, 32), (2, 4))),
        "value_pairs": scatter_about(splits[2], (TOKENS, 2, HEADS * HEAD_DIM), ((8 * TOKENS // HEAD_DIM) ** -0.5), 0.1875, ((0, 32), (2, 4))),
        "init_state": scatter_about(splits[3], (HEADS, HEAD_DIM, HEAD_DIM), 1.0, 6.0, ((0, 4),), jnp.float32),
        "out_weight": scatter_about(splits[4], (HEADS * HEAD_DIM, DMODEL), (HEADS * HEAD_DIM) ** -0.5, 0.125),
    }


epsilon = 1e-06

def product(left, right, pattern):
    return jnp.einsum(pattern, left, right, precision=lax.Precision.HIGHEST)

def unit_rows(entries):
    return entries * lax.rsqrt(lax.optimization_barrier(jnp.sum(entries * entries, axis=-1, keepdims=True)) + epsilon)

def block_parts(query_block, key_block, value_block):
    query_block = unit_rows(query_block.astype(jnp.float32))
    key_block = unit_rows(key_block.astype(jnp.float32))
    value_block = value_block.astype(jnp.float32)
    state_width = key_block.shape[-1]
    micro_len = key_block.shape[-2]
    gram = product(key_block, key_block, '...id,...jd->...ij')
    strict = jnp.tril(jnp.ones((micro_len, micro_len), jnp.float32), -1)
    system = jnp.eye(micro_len, dtype=jnp.float32) + 2.0 * gram * strict
    stacked = 2.0 * jnp.concatenate([key_block, value_block], axis=-1)
    system = jnp.broadcast_to(system, stacked.shape[:-1] + (micro_len,))
    solved = jax.scipy.linalg.solve_triangular(system, stacked, lower=True, unit_diagonal=True)
    writes = solved[..., :state_width]
    updates = solved[..., state_width:]
    scores = product(query_block, key_block, '...id,...jd->...ij')
    row_index = lax.broadcasted_iota(jnp.int32, (query_block.shape[-2], micro_len), 0)
    col_index = lax.broadcasted_iota(jnp.int32, (query_block.shape[-2], micro_len), 1)
    scores = jnp.where(col_index <= 2 * row_index + 1, scores, jnp.zeros_like(scores))
    adjusted = query_block - product(scores, writes, '...ij,...jd->...id')
    inside = product(scores, updates, '...ij,...jd->...id')
    moving = jnp.eye(state_width, dtype=jnp.float32) - product(key_block, writes, '...cd,...ce->...de')
    carried = product(key_block, updates, '...cd,...ce->...de')
    return (adjusted, inside, moving, carried)

def arrange(queries, key_pairs, value_pairs):
    tokens = queries.shape[0]
    head_count = queries.shape[1] // HEAD_DIM
    blocks = tokens // BLOCK
    query_blocks = jnp.transpose(queries.reshape(blocks, BLOCK, head_count, HEAD_DIM), (2, 0, 1, 3))
    key_blocks = jnp.transpose(key_pairs.reshape(blocks, 2 * BLOCK, head_count, HEAD_DIM), (2, 0, 1, 3))
    value_blocks = jnp.transpose(value_pairs.reshape(blocks, 2 * BLOCK, head_count, HEAD_DIM), (2, 0, 1, 3))
    return (query_blocks, key_blocks, value_blocks)

def reference(queries, key_pairs, value_pairs, init_state, out_weight):
    query_blocks, key_blocks, value_blocks = arrange(queries, key_pairs, value_pairs)

    def advance(state, inputs):
        adjusted, inside, moving, carried = block_parts(inputs[0], inputs[1], inputs[2])
        attended = product(adjusted, state, 'hcd,hde->hce') + inside
        following = product(moving, state, 'hij,hjk->hik') + carried
        return (following, attended)
    inputs = (jnp.moveaxis(query_blocks, 1, 0), jnp.moveaxis(key_blocks, 1, 0), jnp.moveaxis(value_blocks, 1, 0))
    final_state, outputs = lax.scan(advance, init_state.astype(jnp.float32), inputs)
    attended = jnp.transpose(outputs, (0, 2, 1, 3)).reshape(TOKENS, HEADS * HEAD_DIM).astype(jnp.bfloat16)
    return jnp.dot(attended.astype(jnp.float32), out_weight.astype(jnp.float32), preferred_element_type=jnp.float32).astype(jnp.bfloat16)
```

```python
import jax
import jax.numpy as jnp
from jax import lax
from jax.sharding import PartitionSpec as P

HEAD_DIM = 128
BLOCK = 32


epsilon = 1e-06


def product(left, right, pattern):
    return jnp.einsum(pattern, left, right, precision=lax.Precision.HIGHEST)


def unit_rows(entries):
    return entries * lax.rsqrt(jnp.sum(entries * entries, axis=-1, keepdims=True) + epsilon)


def unit_lower_inverse(strict):
    size = strict.shape[-1]
    rows = lax.broadcasted_iota(jnp.int32, (size, size), 0)
    cols = lax.broadcasted_iota(jnp.int32, (size, size), 1)
    inverse = jnp.broadcast_to(jnp.eye(size, dtype=jnp.float32), strict.shape)
    width = 1
    while width < size:
        lower_left = (rows // (2 * width) == cols // (2 * width)) & (
            (rows // width) % 2 == 1
        ) & ((cols // width) % 2 == 0)
        coupling = jnp.where(lower_left, strict, 0.0)
        inverse = inverse - product(
            product(inverse, coupling, "...ij,...jk->...ik"), inverse, "...ij,...jk->...ik"
        )
        width *= 2
    return inverse


def block_parts(query_block, key_block, value_block):
    query_block = unit_rows(query_block.astype(jnp.float32))
    key_block = unit_rows(key_block.astype(jnp.float32))
    value_block = value_block.astype(jnp.float32)
    state_width = key_block.shape[-1]
    micro_len = key_block.shape[-2]
    gram = product(key_block, key_block, "...id,...jd->...ij")
    strict = jnp.tril(jnp.ones((micro_len, micro_len), jnp.float32), -1)
    inverse = unit_lower_inverse(2.0 * gram * strict)
    stacked = 2.0 * jnp.concatenate([key_block, value_block], axis=-1)
    solved = product(inverse, stacked, "...ij,...jk->...ik")
    writes = solved[..., :state_width]
    updates = solved[..., state_width:]
    scores = product(query_block, key_block, "...id,...jd->...ij")
    row_index = lax.broadcasted_iota(jnp.int32, (query_block.shape[-2], micro_len), 0)
    col_index = lax.broadcasted_iota(jnp.int32, (query_block.shape[-2], micro_len), 1)
    scores = jnp.where(col_index <= 2 * row_index + 1, scores, jnp.zeros_like(scores))
    adjusted = query_block - product(scores, writes, "...ij,...jd->...id")
    inside = product(scores, updates, "...ij,...jd->...id")
    moving = jnp.eye(state_width, dtype=jnp.float32) - product(
        key_block, writes, "...cd,...ce->...de"
    )
    carried = product(key_block, updates, "...cd,...ce->...de")
    return (adjusted, inside, moving, carried)


def compose(earlier, later):
    return (
        product(later[0], earlier[0], "...ij,...jk->...ik"),
        product(later[0], earlier[1], "...ij,...jk->...ik") + later[1],
    )


def block_prefix(moving, carried):
    count = moving.shape[1]
    identity = jnp.broadcast_to(jnp.eye(moving.shape[-1], dtype=jnp.float32), moving.shape)
    zeros = jnp.zeros_like(carried)
    shift = 1
    while shift < count:
        earlier = (
            jnp.concatenate([identity[:, :shift], moving[:, :-shift]], axis=1),
            jnp.concatenate([zeros[:, :shift], carried[:, :-shift]], axis=1),
        )
        moving, carried = compose(earlier, (moving, carried))
        shift *= 2
    return moving, carried


def shard_prefix(own, axis):
    count = lax.axis_size(axis)
    place = lax.axis_index(axis)
    span = own
    before = (
        jnp.broadcast_to(jnp.eye(own[0].shape[-1], dtype=jnp.float32), own[0].shape),
        jnp.zeros_like(own[1]),
    )
    shift = 1
    while shift < count:
        pairs = [(i, i + shift) for i in range(count - shift)]
        got = jax.tree.map(lambda a: lax.ppermute(a, axis, pairs), span)
        valid = place >= shift
        new_before = compose(got, before)
        before = jax.tree.map(lambda n, o: jnp.where(valid, n, o), new_before, before)
        if 2 * shift < count:
            new_span = compose(got, span)
            span = jax.tree.map(lambda n, o: jnp.where(valid, n, o), new_span, span)
        shift *= 2
    return before


def local(queries, key_pairs, value_pairs, init_state, out_weight):
    tokens = queries.shape[0]
    head_count = queries.shape[1] // HEAD_DIM
    blocks = tokens // BLOCK
    state_width = HEAD_DIM
    query_blocks = jnp.transpose(queries.reshape(blocks, BLOCK, head_count, HEAD_DIM), (2, 0, 1, 3))
    key_blocks = jnp.transpose(
        key_pairs.reshape(blocks, 2 * BLOCK, head_count, HEAD_DIM), (2, 0, 1, 3)
    )
    value_blocks = jnp.transpose(
        value_pairs.reshape(blocks, 2 * BLOCK, head_count, HEAD_DIM), (2, 0, 1, 3)
    )
    adjusted, inside, moving, carried = block_parts(query_blocks, key_blocks, value_blocks)
    prefix_move, prefix_carry = block_prefix(moving, carried)
    shard_map_pair = (prefix_move[:, -1], prefix_carry[:, -1])
    identity = jnp.broadcast_to(
        jnp.eye(state_width, dtype=jnp.float32), (head_count, 1, state_width, state_width)
    )
    start_move = jnp.concatenate([identity, prefix_move[:, :-1]], axis=1)
    start_carry = jnp.concatenate([jnp.zeros_like(identity), prefix_carry[:, :-1]], axis=1)
    query_part = product(adjusted, start_move, "hbcd,hbde->hbce")
    fixed_part = product(adjusted, start_carry, "hbcd,hbde->hbce") + inside
    before_move, before_carry = shard_prefix(shard_map_pair, "seq")
    entering = product(before_move, init_state, "hij,hjk->hik") + before_carry
    attended_heads = product(
        query_part.reshape(head_count, tokens, state_width), entering, "htd,hde->hte"
    ) + fixed_part.reshape(head_count, tokens, state_width)
    attended = (
        jnp.transpose(attended_heads, (1, 0, 2))
        .reshape(tokens, head_count * state_width)
        .astype(jnp.bfloat16)
    )
    groups = lax.axis_size("head")
    group = lax.axis_index("head")
    features = attended.shape[1]
    model_cols = out_weight.shape[1] // groups
    own_cols = lax.dynamic_slice_in_dim(out_weight, group * model_cols, model_cols, 1)

    def partial(block, source):
        rows = lax.dynamic_slice_in_dim(own_cols, source * features, features, 0)
        return jnp.dot(block, rows, preferred_element_type=jnp.float32)

    total = partial(attended, group)
    for offset in range(1, groups):
        pairs = [(i, (i + offset) % groups) for i in range(groups)]
        received = lax.ppermute(attended, "head", pairs)
        total = total + partial(received, (group - offset) % groups)
    return total.astype(jnp.bfloat16)


def solution(mesh):
    in_specs = (
        P("seq", "head"),
        P("seq", None, "head"),
        P("seq", None, "head"),
        P("head", None, None),
        P(),
    )
    out_specs = P("seq", "head")
    return jax.shard_map(local, mesh=mesh, in_specs=in_specs, out_specs=out_specs, check_vma=False)
```

```python
import jax
import jax.numpy as jnp
from jax import lax
from jax.sharding import PartitionSpec as P

HEAD_DIM = 128
BLOCK = 32


epsilon = 1e-06


def product(left, right, pattern):
    return jnp.einsum(pattern, left, right, precision=lax.Precision.HIGHEST)


def unit_rows(entries):
    return entries * lax.rsqrt(jnp.sum(entries * entries, axis=-1, keepdims=True) + epsilon)


def unit_lower_inverse(strict):
    size = strict.shape[-1]
    rows = lax.broadcasted_iota(jnp.int32, (size, size), 0)
    cols = lax.broadcasted_iota(jnp.int32, (size, size), 1)
    inverse = jnp.broadcast_to(jnp.eye(size, dtype=jnp.float32), strict.shape)
    width = 1
    while width < size:
        lower_left = (rows // (2 * width) == cols // (2 * width)) & (
            (rows // width) % 2 == 1
        ) & ((cols // width) % 2 == 0)
        coupling = jnp.where(lower_left, strict, 0.0)
        inverse = inverse - product(
            product(inverse, coupling, "...ij,...jk->...ik"), inverse, "...ij,...jk->...ik"
        )
        width *= 2
    return inverse


def block_parts(query_block, key_block, value_block):
    query_block = unit_rows(query_block.astype(jnp.float32))
    key_block = unit_rows(key_block.astype(jnp.float32))
    value_block = value_block.astype(jnp.float32)
    state_width = key_block.shape[-1]
    micro_len = key_block.shape[-2]
    gram = product(key_block, key_block, "...id,...jd->...ij")
    strict = jnp.tril(jnp.ones((micro_len, micro_len), jnp.float32), -1)
    inverse = unit_lower_inverse(2.0 * gram * strict)
    stacked = 2.0 * jnp.concatenate([key_block, value_block], axis=-1)
    solved = product(inverse, stacked, "...ij,...jk->...ik")
    writes = solved[..., :state_width]
    updates = solved[..., state_width:]
    scores = product(query_block, key_block, "...id,...jd->...ij")
    row_index = lax.broadcasted_iota(jnp.int32, (query_block.shape[-2], micro_len), 0)
    col_index = lax.broadcasted_iota(jnp.int32, (query_block.shape[-2], micro_len), 1)
    scores = jnp.where(col_index <= 2 * row_index + 1, scores, jnp.zeros_like(scores))
    adjusted = query_block - product(scores, writes, "...ij,...jd->...id")
    inside = product(scores, updates, "...ij,...jd->...id")
    moving = jnp.eye(state_width, dtype=jnp.float32) - product(
        key_block, writes, "...cd,...ce->...de"
    )
    carried = product(key_block, updates, "...cd,...ce->...de")
    return (adjusted, inside, moving, carried)


def compose(earlier, later):
    width = later.shape[-2]
    moved = product(later[..., :width], earlier, "...ij,...jk->...ik")
    return moved + jnp.concatenate([jnp.zeros_like(later[..., :width]), later[..., width:]], axis=-1)


def identity_map(shape):
    width = shape[-2]
    eye = jnp.concatenate(
        [jnp.eye(width, dtype=jnp.float32), jnp.zeros((width, width), jnp.float32)], axis=-1
    )
    return jnp.broadcast_to(eye, shape)


def block_prefix(maps):
    count = maps.shape[1]
    identity = identity_map(maps.shape)
    shift = 1
    while shift < count:
        earlier = jnp.concatenate([identity[:, :shift], maps[:, :-shift]], axis=1)
        maps = compose(earlier, maps)
        shift *= 2
    return maps


def block_total(maps):
    while maps.shape[1] > 1:
        maps = compose(maps[:, 0::2], maps[:, 1::2])
    return maps[:, 0]


def shard_prefix(own, axis, radix=4):
    count = lax.axis_size(axis)
    place = lax.axis_index(axis)
    identity = identity_map(own.shape)
    span = own
    before = identity
    unit = 1
    while unit < count:
        got = []
        for step in range(1, radix):
            distance = step * unit
            if distance >= count:
                break
            pairs = [(i, i + distance) for i in range(count - distance)]
            received = lax.ppermute(span, axis, pairs)
            got.append(jnp.where(place >= distance, received, identity))
        joined = got[-1]
        for piece in reversed(got[:-1]):
            joined = compose(joined, piece)
        before = compose(joined, before)
        if unit * radix < count:
            span = compose(joined, span)
        unit *= radix
    return before


def local(queries, key_pairs, value_pairs, init_state, out_weight):
    tokens = queries.shape[0]
    head_count = queries.shape[1] // HEAD_DIM
    blocks = tokens // BLOCK
    state_width = HEAD_DIM
    query_blocks = jnp.transpose(queries.reshape(blocks, BLOCK, head_count, HEAD_DIM), (2, 0, 1, 3))
    key_blocks = jnp.transpose(
        key_pairs.reshape(blocks, 2 * BLOCK, head_count, HEAD_DIM), (2, 0, 1, 3)
    )
    value_blocks = jnp.transpose(
        value_pairs.reshape(blocks, 2 * BLOCK, head_count, HEAD_DIM), (2, 0, 1, 3)
    )
    adjusted, inside, moving, carried = block_parts(query_blocks, key_blocks, value_blocks)
    maps = jnp.concatenate([moving, carried], axis=-1)
    before = shard_prefix(block_total(maps), "seq")
    entering = product(before[..., :state_width], init_state, "hij,hjk->hik") + before[..., state_width:]
    prefix = block_prefix(maps)
    start = jnp.concatenate([identity_map(prefix[:, :1].shape), prefix[:, :-1]], axis=1)
    start_map = product(adjusted, start, "hbcd,hbde->hbce")
    query_part = start_map[..., :state_width]
    fixed_part = start_map[..., state_width:] + inside
    attended_heads = product(
        query_part.reshape(head_count, tokens, state_width), entering, "htd,hde->hte"
    ) + fixed_part.reshape(head_count, tokens, state_width)
    attended = (
        jnp.transpose(attended_heads, (1, 0, 2))
        .reshape(tokens, head_count * state_width)
        .astype(jnp.bfloat16)
    )
    groups = lax.axis_size("head")
    group = lax.axis_index("head")
    features = attended.shape[1]
    model_cols = out_weight.shape[1] // groups
    own_cols = lax.dynamic_slice_in_dim(out_weight, group * model_cols, model_cols, 1)

    def partial(block, source):
        rows = lax.dynamic_slice_in_dim(own_cols, source * features, features, 0)
        return jnp.dot(block, rows, preferred_element_type=jnp.float32)

    total = partial(attended, group)
    for offset in range(1, groups):
        pairs = [(i, (i + offset) % groups) for i in range(groups)]
        received = lax.ppermute(attended, "head", pairs)
        total = total + partial(received, (group - offset) % groups)
    return total.astype(jnp.bfloat16)


def solution(mesh):
    in_specs = (
        P("seq", "head"),
        P("seq", None, "head"),
        P("seq", None, "head"),
        P("head", None, None),
        P(),
    )
    out_specs = P("seq", "head")
    return jax.shard_map(local, mesh=mesh, in_specs=in_specs, out_specs=out_specs, check_vma=False)
```

```python
import jax
import jax.numpy as jnp
from jax import lax
from jax.sharding import PartitionSpec as P

HEAD_DIM = 128
BLOCK = 32


epsilon = 1e-06


def product(left, right, pattern):
    return jnp.einsum(pattern, left, right, precision=lax.Precision.HIGH)


def unit_rows(entries):
    return entries * lax.rsqrt(jnp.sum(entries * entries, axis=-1, keepdims=True) + epsilon)


def unit_lower_inverse(strict):
    size = strict.shape[-1]
    rows = lax.broadcasted_iota(jnp.int32, (size, size), 0)
    cols = lax.broadcasted_iota(jnp.int32, (size, size), 1)
    inverse = jnp.broadcast_to(jnp.eye(size, dtype=jnp.float32), strict.shape)
    width = 1
    while width < size:
        lower_left = (rows // (2 * width) == cols // (2 * width)) & (
            (rows // width) % 2 == 1
        ) & ((cols // width) % 2 == 0)
        coupling = jnp.where(lower_left, strict, 0.0)
        inverse = inverse - product(
            product(inverse, coupling, "...ij,...jk->...ik"), inverse, "...ij,...jk->...ik"
        )
        width *= 2
    return inverse


def block_parts(query_block, key_block, value_block):
    query_block = unit_rows(query_block.astype(jnp.float32))
    key_block = unit_rows(key_block.astype(jnp.float32))
    value_block = value_block.astype(jnp.float32)
    state_width = key_block.shape[-1]
    micro_len = key_block.shape[-2]
    gram = product(key_block, key_block, "...id,...jd->...ij")
    strict = jnp.tril(jnp.ones((micro_len, micro_len), jnp.float32), -1)
    inverse = unit_lower_inverse(2.0 * gram * strict)
    stacked = 2.0 * jnp.concatenate([key_block, value_block], axis=-1)
    solved = product(inverse, stacked, "...ij,...jk->...ik")
    writes = solved[..., :state_width]
    updates = solved[..., state_width:]
    scores = product(query_block, key_block, "...id,...jd->...ij")
    row_index = lax.broadcasted_iota(jnp.int32, (query_block.shape[-2], micro_len), 0)
    col_index = lax.broadcasted_iota(jnp.int32, (query_block.shape[-2], micro_len), 1)
    scores = jnp.where(col_index <= 2 * row_index + 1, scores, jnp.zeros_like(scores))
    adjusted = query_block - product(scores, writes, "...ij,...jd->...id")
    inside = product(scores, updates, "...ij,...jd->...id")
    moving = jnp.eye(state_width, dtype=jnp.float32) - product(
        key_block, writes, "...cd,...ce->...de"
    )
    carried = product(key_block, updates, "...cd,...ce->...de")
    return (adjusted, inside, moving, carried)


def compose(earlier, later):
    return (
        product(later[0], earlier[0], "...ij,...jk->...ik"),
        product(later[0], earlier[1], "...ij,...jk->...ik") + later[1],
    )


def identity_map(shape):
    eye = jnp.broadcast_to(jnp.eye(shape[-1], dtype=jnp.float32), shape)
    return (eye, jnp.zeros(shape, jnp.float32))


def block_prefix(maps):
    count = maps[0].shape[1]
    identity = identity_map(maps[0].shape)
    shift = 1
    while shift < count:
        earlier = jax.tree.map(
            lambda e, a: jnp.concatenate([e[:, :shift], a[:, :-shift]], axis=1), identity, maps
        )
        maps = compose(earlier, maps)
        shift *= 2
    return maps


def block_total(maps):
    while maps[0].shape[1] > 1:
        paired = jax.tree.map(lambda a: a.reshape((a.shape[0], -1, 2) + a.shape[2:]), maps)
        maps = compose(
            jax.tree.map(lambda a: a[:, :, 0], paired), jax.tree.map(lambda a: a[:, :, 1], paired)
        )
    return jax.tree.map(lambda a: a[:, 0], maps)


def shard_prefix(own, axis, radix=4):
    count = lax.axis_size(axis)
    place = lax.axis_index(axis)
    identity = identity_map(own[0].shape)
    span = own
    before = identity
    unit = 1
    while unit < count:
        got = []
        for step in range(1, radix):
            distance = step * unit
            if distance >= count:
                break
            pairs = [(i, i + distance) for i in range(count - distance)]
            valid = place >= distance
            got.append(
                jax.tree.map(
                    lambda a, e: jnp.where(valid, lax.ppermute(a, axis, pairs), e), span, identity
                )
            )
        joined = got[-1]
        for piece in reversed(got[:-1]):
            joined = compose(joined, piece)
        before = compose(joined, before)
        if unit * radix < count:
            span = compose(joined, span)
        unit *= radix
    return before


def local(queries, key_pairs, value_pairs, init_state, out_weight):
    tokens = queries.shape[0]
    head_count = queries.shape[1] // HEAD_DIM
    blocks = tokens // BLOCK
    state_width = HEAD_DIM
    query_blocks = jnp.transpose(queries.reshape(blocks, BLOCK, head_count, HEAD_DIM), (2, 0, 1, 3))
    key_blocks = jnp.transpose(
        key_pairs.reshape(blocks, 2 * BLOCK, head_count, HEAD_DIM), (2, 0, 1, 3)
    )
    value_blocks = jnp.transpose(
        value_pairs.reshape(blocks, 2 * BLOCK, head_count, HEAD_DIM), (2, 0, 1, 3)
    )
    adjusted, inside, moving, carried = block_parts(query_blocks, key_blocks, value_blocks)
    maps = (moving, carried)
    before_move, before_carry = shard_prefix(block_total(maps), "seq")
    entering = product(before_move, init_state, "hij,hjk->hik") + before_carry
    prefix_move, prefix_carry = block_prefix(maps)
    identity = identity_map(prefix_move[:, :1].shape)
    start_move = jnp.concatenate([identity[0], prefix_move[:, :-1]], axis=1)
    start_carry = jnp.concatenate([identity[1], prefix_carry[:, :-1]], axis=1)
    query_part = product(adjusted, start_move, "hbcd,hbde->hbce")
    fixed_part = product(adjusted, start_carry, "hbcd,hbde->hbce") + inside
    attended_heads = product(
        query_part.reshape(head_count, tokens, state_width), entering, "htd,hde->hte"
    ) + fixed_part.reshape(head_count, tokens, state_width)
    attended = (
        jnp.transpose(attended_heads, (1, 0, 2))
        .reshape(tokens, head_count * state_width)
        .astype(jnp.bfloat16)
    )
    groups = lax.axis_size("head")
    group = lax.axis_index("head")
    features = attended.shape[1]
    model_cols = out_weight.shape[1] // groups
    own_cols = lax.dynamic_slice_in_dim(out_weight, group * model_cols, model_cols, 1)

    def partial(block, source):
        rows = lax.dynamic_slice_in_dim(own_cols, source * features, features, 0)
        return jnp.dot(block, rows, preferred_element_type=jnp.float32)

    total = partial(attended, group)
    for offset in range(1, groups):
        pairs = [(i, (i + offset) % groups) for i in range(groups)]
        received = lax.ppermute(attended, "head", pairs)
        total = total + partial(received, (group - offset) % groups)
    return total.astype(jnp.bfloat16)


def solution(mesh):
    in_specs = (
        P("seq", "head"),
        P("seq", None, "head"),
        P("seq", None, "head"),
        P("head", None, None),
        P(),
    )
    out_specs = P("seq", "head")
    return jax.shard_map(local, mesh=mesh, in_specs=in_specs, out_specs=out_specs, check_vma=False)
```

```python
import jax
import jax.numpy as jnp
from jax import lax
from jax.sharding import PartitionSpec as P

HEAD_DIM = 128
BLOCK = 32


epsilon = 1e-06


def product(left, right, pattern):
    return jnp.einsum(pattern, left, right, precision=lax.Precision.HIGHEST)


def unit_rows(entries):
    return entries * lax.rsqrt(jnp.sum(entries * entries, axis=-1, keepdims=True) + epsilon)


def unit_lower_inverse(strict):
    size = strict.shape[-1]
    rows = lax.broadcasted_iota(jnp.int32, (size, size), 0)
    cols = lax.broadcasted_iota(jnp.int32, (size, size), 1)
    inverse = jnp.broadcast_to(jnp.eye(size, dtype=jnp.float32), strict.shape)
    width = 1
    while width < size:
        lower_left = (rows // (2 * width) == cols // (2 * width)) & (
            (rows // width) % 2 == 1
        ) & ((cols // width) % 2 == 0)
        coupling = jnp.where(lower_left, strict, 0.0)
        inverse = inverse - product(
            product(inverse, coupling, "...ij,...jk->...ik"), inverse, "...ij,...jk->...ik"
        )
        width *= 2
    return inverse


def block_parts(query_block, key_block, value_block):
    query_block = unit_rows(query_block.astype(jnp.float32))
    key_block = unit_rows(key_block.astype(jnp.float32))
    value_block = value_block.astype(jnp.float32)
    state_width = key_block.shape[-1]
    micro_len = key_block.shape[-2]
    gram = product(key_block, key_block, "...id,...jd->...ij")
    strict = jnp.tril(jnp.ones((micro_len, micro_len), jnp.float32), -1)
    inverse = unit_lower_inverse(2.0 * gram * strict)
    stacked = 2.0 * jnp.concatenate([key_block, value_block], axis=-1)
    solved = product(inverse, stacked, "...ij,...jk->...ik")
    writes = solved[..., :state_width]
    updates = solved[..., state_width:]
    scores = product(query_block, key_block, "...id,...jd->...ij")
    row_index = lax.broadcasted_iota(jnp.int32, (query_block.shape[-2], micro_len), 0)
    col_index = lax.broadcasted_iota(jnp.int32, (query_block.shape[-2], micro_len), 1)
    scores = jnp.where(col_index <= 2 * row_index + 1, scores, jnp.zeros_like(scores))
    adjusted = query_block - product(scores, writes, "...ij,...jd->...id")
    inside = product(scores, updates, "...ij,...jd->...id")
    moving = jnp.eye(state_width, dtype=jnp.float32) - product(
        key_block, writes, "...cd,...ce->...de"
    )
    carried = product(key_block, updates, "...cd,...ce->...de")
    return (adjusted, inside, moving, carried)


def compose(earlier, later):
    return (
        product(later[0], earlier[0], "...ij,...jk->...ik"),
        product(later[0], earlier[1], "...ij,...jk->...ik") + later[1],
    )


def block_prefix(moving, carried):
    count = moving.shape[1]
    identity = jnp.broadcast_to(jnp.eye(moving.shape[-1], dtype=jnp.float32), moving.shape)
    zeros = jnp.zeros_like(carried)
    shift = 1
    while shift < count:
        earlier = (
            jnp.concatenate([identity[:, :shift], moving[:, :-shift]], axis=1),
            jnp.concatenate([zeros[:, :shift], carried[:, :-shift]], axis=1),
        )
        moving, carried = compose(earlier, (moving, carried))
        shift *= 2
    return moving, carried


def shard_prefix(own, axis):
    count = lax.axis_size(axis)
    place = lax.axis_index(axis)
    span = own
    before = (
        jnp.broadcast_to(jnp.eye(own[0].shape[-1], dtype=jnp.float32), own[0].shape),
        jnp.zeros_like(own[1]),
    )
    shift = 1
    while shift < count:
        pairs = [(i, i + shift) for i in range(count - shift)]
        packed = lax.ppermute(jnp.concatenate(span, axis=-1), axis, pairs)
        width = span[0].shape[-1]
        got = (packed[..., :width], packed[..., width:])
        valid = place >= shift
        new_before = compose(got, before)
        before = jax.tree.map(lambda n, o: jnp.where(valid, n, o), new_before, before)
        if 2 * shift < count:
            new_span = compose(got, span)
            span = jax.tree.map(lambda n, o: jnp.where(valid, n, o), new_span, span)
        shift *= 2
    return before


def local(queries, key_pairs, value_pairs, init_state, out_weight):
    tokens = queries.shape[0]
    head_count = queries.shape[1] // HEAD_DIM
    blocks = tokens // BLOCK
    state_width = HEAD_DIM
    query_blocks = jnp.transpose(queries.reshape(blocks, BLOCK, head_count, HEAD_DIM), (2, 0, 1, 3))
    key_blocks = jnp.transpose(
        key_pairs.reshape(blocks, 2 * BLOCK, head_count, HEAD_DIM), (2, 0, 1, 3)
    )
    value_blocks = jnp.transpose(
        value_pairs.reshape(blocks, 2 * BLOCK, head_count, HEAD_DIM), (2, 0, 1, 3)
    )
    adjusted, inside, moving, carried = block_parts(query_blocks, key_blocks, value_blocks)
    prefix_move, prefix_carry = block_prefix(moving, carried)
    shard_map_pair = (prefix_move[:, -1], prefix_carry[:, -1])
    identity = jnp.broadcast_to(
        jnp.eye(state_width, dtype=jnp.float32), (head_count, 1, state_width, state_width)
    )
    start_move = jnp.concatenate([identity, prefix_move[:, :-1]], axis=1)
    start_carry = jnp.concatenate([jnp.zeros_like(identity), prefix_carry[:, :-1]], axis=1)
    query_part = product(adjusted, start_move, "hbcd,hbde->hbce")
    fixed_part = product(adjusted, start_carry, "hbcd,hbde->hbce") + inside
    before_move, before_carry = shard_prefix(shard_map_pair, "seq")
    entering = product(before_move, init_state, "hij,hjk->hik") + before_carry
    attended_heads = product(
        query_part.reshape(head_count, tokens, state_width), entering, "htd,hde->hte"
    ) + fixed_part.reshape(head_count, tokens, state_width)
    attended = (
        jnp.transpose(attended_heads, (1, 0, 2))
        .reshape(tokens, head_count * state_width)
        .astype(jnp.bfloat16)
    )
    groups = lax.axis_size("head")
    group = lax.axis_index("head")
    features = attended.shape[1]
    model_cols = out_weight.shape[1] // groups
    own_cols = lax.dynamic_slice_in_dim(out_weight, group * model_cols, model_cols, 1)

    def partial(block, source):
        rows = lax.dynamic_slice_in_dim(own_cols, source * features, features, 0)
        return jnp.dot(block, rows, preferred_element_type=jnp.float32)

    total = partial(attended, group)
    for offset in range(1, groups):
        pairs = [(i, (i + offset) % groups) for i in range(groups)]
        received = lax.ppermute(attended, "head", pairs)
        total = total + partial(received, (group - offset) % groups)
    return total.astype(jnp.bfloat16)


def solution(mesh):
    in_specs = (
        P("seq", "head"),
        P("seq", None, "head"),
        P("seq", None, "head"),
        P("head", None, None),
        P(),
    )
    out_specs = P("seq", "head")
    return jax.shard_map(local, mesh=mesh, in_specs=in_specs, out_specs=out_specs, check_vma=False)
```

```python
import jax
import jax.numpy as jnp
from jax import lax
from jax.sharding import PartitionSpec as P

HEAD_DIM = 128
BLOCK = 32


epsilon = 1e-06


def product(left, right, pattern):
    return jnp.einsum(pattern, left, right, precision=lax.Precision.HIGHEST)


def unit_rows(entries):
    return entries * lax.rsqrt(jnp.sum(entries * entries, axis=-1, keepdims=True) + epsilon)


def unit_lower_inverse(strict):
    size = strict.shape[-1]
    rows = lax.broadcasted_iota(jnp.int32, (size, size), 0)
    cols = lax.broadcasted_iota(jnp.int32, (size, size), 1)
    inverse = jnp.broadcast_to(jnp.eye(size, dtype=jnp.float32), strict.shape)
    width = 1
    while width < size:
        lower_left = (rows // (2 * width) == cols // (2 * width)) & (
            (rows // width) % 2 == 1
        ) & ((cols // width) % 2 == 0)
        coupling = jnp.where(lower_left, strict, 0.0)
        inverse = inverse - product(
            product(inverse, coupling, "...ij,...jk->...ik"), inverse, "...ij,...jk->...ik"
        )
        width *= 2
    return inverse


def block_parts(query_block, key_block, value_block):
    query_block = unit_rows(query_block.astype(jnp.float32))
    key_block = unit_rows(key_block.astype(jnp.float32))
    value_block = value_block.astype(jnp.float32)
    state_width = key_block.shape[-1]
    micro_len = key_block.shape[-2]
    gram = product(key_block, key_block, "...id,...jd->...ij")
    strict = jnp.tril(jnp.ones((micro_len, micro_len), jnp.float32), -1)
    inverse = unit_lower_inverse(2.0 * gram * strict)
    stacked = 2.0 * jnp.concatenate([key_block, value_block], axis=-1)
    solved = product(inverse, stacked, "...ij,...jk->...ik")
    writes = solved[..., :state_width]
    updates = solved[..., state_width:]
    scores = product(query_block, key_block, "...id,...jd->...ij")
    row_index = lax.broadcasted_iota(jnp.int32, (query_block.shape[-2], micro_len), 0)
    col_index = lax.broadcasted_iota(jnp.int32, (query_block.shape[-2], micro_len), 1)
    scores = jnp.where(col_index <= 2 * row_index + 1, scores, jnp.zeros_like(scores))
    adjusted = query_block - product(scores, writes, "...ij,...jd->...id")
    inside = product(scores, updates, "...ij,...jd->...id")
    moving = jnp.eye(state_width, dtype=jnp.float32) - product(
        key_block, writes, "...cd,...ce->...de"
    )
    carried = product(key_block, updates, "...cd,...ce->...de")
    return (adjusted, inside, moving, carried)


def compose(earlier, later):
    return (
        product(later[0], earlier[0], "...ij,...jk->...ik"),
        product(later[0], earlier[1], "...ij,...jk->...ik") + later[1],
    )


def block_prefix(moving, carried):
    count = moving.shape[1]
    shift = 1
    while shift < count:
        new_move, new_carry = compose(
            (moving[:, :-shift], carried[:, :-shift]), (moving[:, shift:], carried[:, shift:])
        )
        moving = jnp.concatenate([moving[:, :shift], new_move], axis=1)
        carried = jnp.concatenate([carried[:, :shift], new_carry], axis=1)
        shift *= 2
    return moving, carried


def shard_prefix(own, axis):
    count = lax.axis_size(axis)
    place = lax.axis_index(axis)
    span = own
    before = (
        jnp.broadcast_to(jnp.eye(own[0].shape[-1], dtype=jnp.float32), own[0].shape),
        jnp.zeros_like(own[1]),
    )
    shift = 1
    while shift < count:
        pairs = [(i, i + shift) for i in range(count - shift)]
        got = jax.tree.map(lambda a: lax.ppermute(a, axis, pairs), span)
        valid = place >= shift
        new_before = got if shift == 1 else compose(got, before)
        before = jax.tree.map(lambda n, o: jnp.where(valid, n, o), new_before, before)
        if 2 * shift < count:
            new_span = compose(got, span)
            span = jax.tree.map(lambda n, o: jnp.where(valid, n, o), new_span, span)
        shift *= 2
    return before


def local(queries, key_pairs, value_pairs, init_state, out_weight):
    tokens = queries.shape[0]
    head_count = queries.shape[1] // HEAD_DIM
    blocks = tokens // BLOCK
    state_width = HEAD_DIM
    query_blocks = jnp.transpose(queries.reshape(blocks, BLOCK, head_count, HEAD_DIM), (2, 0, 1, 3))
    key_blocks = jnp.transpose(
        key_pairs.reshape(blocks, 2 * BLOCK, head_count, HEAD_DIM), (2, 0, 1, 3)
    )
    value_blocks = jnp.transpose(
        value_pairs.reshape(blocks, 2 * BLOCK, head_count, HEAD_DIM), (2, 0, 1, 3)
    )
    adjusted, inside, moving, carried = block_parts(query_blocks, key_blocks, value_blocks)
    prefix_move, prefix_carry = block_prefix(moving, carried)
    shard_map_pair = (prefix_move[:, -1], prefix_carry[:, -1])
    identity = jnp.broadcast_to(
        jnp.eye(state_width, dtype=jnp.float32), (head_count, 1, state_width, state_width)
    )
    start_move = jnp.concatenate([identity, prefix_move[:, :-1]], axis=1)
    start_carry = jnp.concatenate([jnp.zeros_like(identity), prefix_carry[:, :-1]], axis=1)
    query_part = product(adjusted, start_move, "hbcd,hbde->hbce")
    fixed_part = product(adjusted, start_carry, "hbcd,hbde->hbce") + inside
    before_move, before_carry = shard_prefix(shard_map_pair, "seq")
    entering = product(before_move, init_state, "hij,hjk->hik") + before_carry
    attended_heads = product(
        query_part.reshape(head_count, tokens, state_width), entering, "htd,hde->hte"
    ) + fixed_part.reshape(head_count, tokens, state_width)
    attended = (
        jnp.transpose(attended_heads, (1, 0, 2))
        .reshape(tokens, head_count * state_width)
        .astype(jnp.bfloat16)
    )
    groups = lax.axis_size("head")
    group = lax.axis_index("head")
    features = attended.shape[1]
    model_cols = out_weight.shape[1] // groups
    own_cols = lax.dynamic_slice_in_dim(out_weight, group * model_cols, model_cols, 1)

    def partial(block, source):
        rows = lax.dynamic_slice_in_dim(own_cols, source * features, features, 0)
        return jnp.dot(block, rows, preferred_element_type=jnp.float32)

    total = partial(attended, group)
    for offset in range(1, groups):
        pairs = [(i, (i + offset) % groups) for i in range(groups)]
        received = lax.ppermute(attended, "head", pairs)
        total = total + partial(received, (group - offset) % groups)
    return total.astype(jnp.bfloat16)


def solution(mesh):
    in_specs = (
        P("seq", "head"),
        P("seq", None, "head"),
        P("seq", None, "head"),
        P("head", None, None),
        P(),
    )
    out_specs = P("seq", "head")
    return jax.shard_map(local, mesh=mesh, in_specs=in_specs, out_specs=out_specs, check_vma=False)
```

```python
import jax
import jax.numpy as jnp
from jax import lax
from jax.sharding import PartitionSpec as P

HEAD_DIM = 128
BLOCK = 32


epsilon = 1e-06


def product(left, right, pattern):
    return jnp.einsum(pattern, left, right, precision=lax.Precision.HIGHEST)


def unit_rows(entries):
    return entries * lax.rsqrt(jnp.sum(entries * entries, axis=-1, keepdims=True) + epsilon)


def unit_lower_inverse(strict):
    size = strict.shape[-1]
    rows = lax.broadcasted_iota(jnp.int32, (size, size), 0)
    cols = lax.broadcasted_iota(jnp.int32, (size, size), 1)
    inverse = jnp.broadcast_to(jnp.eye(size, dtype=jnp.float32), strict.shape)
    width = 1
    while width < size:
        lower_left = (rows // (2 * width) == cols // (2 * width)) & (
            (rows // width) % 2 == 1
        ) & ((cols // width) % 2 == 0)
        coupling = jnp.where(lower_left, strict, 0.0)
        if width == 1:
            inverse = inverse - coupling
        else:
            inverse = inverse - product(
                product(inverse, coupling, "...ij,...jk->...ik"), inverse, "...ij,...jk->...ik"
            )
        width *= 2
    return inverse


def block_parts(query_block, key_block, value_block):
    query_block = unit_rows(query_block.astype(jnp.float32))
    key_block = unit_rows(key_block.astype(jnp.float32))
    value_block = value_block.astype(jnp.float32)
    state_width = key_block.shape[-1]
    micro_len = key_block.shape[-2]
    gram = product(key_block, key_block, "...id,...jd->...ij")
    strict = jnp.tril(jnp.ones((micro_len, micro_len), jnp.float32), -1)
    inverse = unit_lower_inverse(2.0 * gram * strict)
    stacked = 2.0 * jnp.concatenate([key_block, value_block], axis=-1)
    solved = product(inverse, stacked, "...ij,...jk->...ik")
    writes = solved[..., :state_width]
    updates = solved[..., state_width:]
    scores = product(query_block, key_block, "...id,...jd->...ij")
    row_index = lax.broadcasted_iota(jnp.int32, (query_block.shape[-2], micro_len), 0)
    col_index = lax.broadcasted_iota(jnp.int32, (query_block.shape[-2], micro_len), 1)
    scores = jnp.where(col_index <= 2 * row_index + 1, scores, jnp.zeros_like(scores))
    adjusted = query_block - product(scores, writes, "...ij,...jd->...id")
    inside = product(scores, updates, "...ij,...jd->...id")
    moving = jnp.eye(state_width, dtype=jnp.float32) - product(
        key_block, writes, "...cd,...ce->...de"
    )
    carried = product(key_block, updates, "...cd,...ce->...de")
    return (adjusted, inside, moving, carried)


def compose(earlier, later):
    return (
        product(later[0], earlier[0], "...ij,...jk->...ik"),
        product(later[0], earlier[1], "...ij,...jk->...ik") + later[1],
    )


def block_prefix(moving, carried):
    count = moving.shape[1]
    shift = 1
    while shift < count:
        new_move, new_carry = compose(
            (moving[:, :-shift], carried[:, :-shift]), (moving[:, shift:], carried[:, shift:])
        )
        moving = jnp.concatenate([moving[:, :shift], new_move], axis=1)
        carried = jnp.concatenate([carried[:, :shift], new_carry], axis=1)
        shift *= 2
    return moving, carried


def shard_prefix(own, axis):
    count = lax.axis_size(axis)
    place = lax.axis_index(axis)
    span = own
    before = (
        jnp.broadcast_to(jnp.eye(own[0].shape[-1], dtype=jnp.float32), own[0].shape),
        jnp.zeros_like(own[1]),
    )
    shift = 1
    while shift < count:
        pairs = [(i, i + shift) for i in range(count - shift)]
        got = jax.tree.map(lambda a: lax.ppermute(a, axis, pairs), span)
        valid = place >= shift
        new_before = got if shift == 1 else compose(got, before)
        before = jax.tree.map(lambda n, o: jnp.where(valid, n, o), new_before, before)
        if 2 * shift < count:
            new_span = compose(got, span)
            span = jax.tree.map(lambda n, o: jnp.where(valid, n, o), new_span, span)
        shift *= 2
    return before


def local(queries, key_pairs, value_pairs, init_state, out_weight):
    tokens = queries.shape[0]
    head_count = queries.shape[1] // HEAD_DIM
    blocks = tokens // BLOCK
    state_width = HEAD_DIM
    query_blocks = jnp.transpose(queries.reshape(blocks, BLOCK, head_count, HEAD_DIM), (2, 0, 1, 3))
    key_blocks = jnp.transpose(
        key_pairs.reshape(blocks, 2 * BLOCK, head_count, HEAD_DIM), (2, 0, 1, 3)
    )
    value_blocks = jnp.transpose(
        value_pairs.reshape(blocks, 2 * BLOCK, head_count, HEAD_DIM), (2, 0, 1, 3)
    )
    adjusted, inside, moving, carried = block_parts(query_blocks, key_blocks, value_blocks)
    prefix_move, prefix_carry = block_prefix(moving, carried)
    shard_map_pair = (prefix_move[:, -1], prefix_carry[:, -1])
    identity = jnp.broadcast_to(
        jnp.eye(state_width, dtype=jnp.float32), (head_count, 1, state_width, state_width)
    )
    start_move = jnp.concatenate([identity, prefix_move[:, :-1]], axis=1)
    start_carry = jnp.concatenate([jnp.zeros_like(identity), prefix_carry[:, :-1]], axis=1)
    query_part = product(adjusted, start_move, "hbcd,hbde->hbce")
    fixed_part = product(adjusted, start_carry, "hbcd,hbde->hbce") + inside
    before_move, before_carry = shard_prefix(shard_map_pair, "seq")
    entering = product(before_move, init_state, "hij,hjk->hik") + before_carry
    attended_heads = product(
        query_part.reshape(head_count, tokens, state_width), entering, "htd,hde->hte"
    ) + fixed_part.reshape(head_count, tokens, state_width)
    attended = (
        jnp.transpose(attended_heads, (1, 0, 2))
        .reshape(tokens, head_count * state_width)
        .astype(jnp.bfloat16)
    )
    groups = lax.axis_size("head")
    group = lax.axis_index("head")
    features = attended.shape[1]
    model_cols = out_weight.shape[1] // groups
    own_cols = lax.dynamic_slice_in_dim(out_weight, group * model_cols, model_cols, 1)

    def partial(block, source):
        rows = lax.dynamic_slice_in_dim(own_cols, source * features, features, 0)
        return jnp.dot(block, rows, preferred_element_type=jnp.float32)

    total = partial(attended, group)
    for offset in range(1, groups):
        pairs = [(i, (i + offset) % groups) for i in range(groups)]
        received = lax.ppermute(attended, "head", pairs)
        total = total + partial(received, (group - offset) % groups)
    return total.astype(jnp.bfloat16)


def solution(mesh):
    in_specs = (
        P("seq", "head"),
        P("seq", None, "head"),
        P("seq", None, "head"),
        P("head", None, None),
        P(),
    )
    out_specs = P("seq", "head")
    return jax.shard_map(local, mesh=mesh, in_specs=in_specs, out_specs=out_specs, check_vma=False)
```
